1024 devices in a mesh: dp: 64 (over z, core), expert: 16 (over y, x).
Axes of the slice: x: 4, y: 4, z: 32, core: 2. Of those that a mesh axis runs over, the one named last changes fastest.
Arguments:
- tokens: bfloat16 [131072, 2048], P(('dp', 'expert')), may hold values from -6 to 6
- upstream: bfloat16 [131072, 2048], P(('dp', 'expert')), may hold values from -6 to 6
- expert_ids: int32 [131072, 8], P(('dp', 'expert')), may hold values from 0 to 127, all different within a row; in each aligned block of 128 rows (0 to 127, 128 to 255, ...) at most 10 rows name the same one
- gate_weights: bfloat16 [131072, 8], P(('dp', 'expert')), may hold values from 0.049804688 to 0.5
- w_up: bfloat16 [16, 2048, 768], P('expert'), may hold values from -0.125 to 0.125
- w_down: bfloat16 [16, 768, 2048], P('expert'), may hold values from -0.21875 to 0.21875
Outputs:
- token_grads: bfloat16 [131072, 2048], P(('dp', 'expert'))
- gate_grads: bfloat16 [131072, 8], P(('dp', 'expert'))
- router_grads: float32 [16, 2048], P('expert')
The draws below stay inside these ranges and needn't reach their ends.
Inputs may be any that keep to these rules, and one draw needn't show every extreme that they name: `expert_ids`: each row names 8 different experts; among the 128 rows of one device no expert is named by more than 10 rows.
All inputs are finite; a program needn't handle non-finite values.
Results may differ from the reference program's by a relative error of at most 0.0063.
Values may be sent and summed in bfloat16 or wider, within the bound.
No kernel may reach another device: no remote copies, remote signals or barrier semaphores. Data moves between devices by JAX's collectives and lax.ppermute only.
A program may use at most 32 MiB of HBM per device.

```python
import math
import jax
import jax.numpy as jnp
import numpy as np
from jax import lax

D = 2048
F = 768
TOP = 8
EXP_DEV = 8
TOK_DEV = 128
EXPERTS = 128
FLIGHTS = 16
MOST = 10
COLUMN_TOK = 8192
TOKENS = 131072
N_DP = 64
N_EXPERT = 16


def block_levels(rng, dims, cuts, low, top_value):
    loudness = 1.0
    for dim, shards_of in cuts:
        draws = jax.random.uniform(jax.random.fold_in(jax.random.fold_in(rng, 6), dim), (shards_of,), jnp.float32, low / len(cuts), top_value / len(cuts))
        loudness = loudness * jnp.repeat(jnp.exp(draws), dims[dim] // shards_of).reshape((-1,) + (1,) * (len(dims) - 1 - dim))
    return loudness


def shared_out(key, own, number, rows, amount, top, bound, slope):
    ranking = jax.random.permutation(key, amount)
    crowded, usual = portions_of(amount, rows * top, bound, slope, True), portions_of(amount, rows * top, bound, slope, False)
    places = jnp.arange(amount)

    def named(tallies, offset_by):
        used = int((tallies > 0).sum())
        fixed = max(1, used // 4)
        passed = fixed + (places - fixed + offset_by * (used - fixed)) % max(1, amount - fixed)
        return jnp.zeros((amount,), jnp.int32).at[ranking[jnp.where(places < fixed, places, passed)]].set(jnp.asarray(tallies, jnp.int32))

    tallies = jnp.where(number % 4 == 0, named(crowded, number // 4), named(usual, number - number // 4 - 1))
    mixed = jax.random.permutation(jax.random.fold_in(own, 3), amount)
    source_of, sink = mixed[0:amount // 2 * 2:2], mixed[1:amount // 2 * 2:2]
    margin = jnp.minimum(tallies[source_of] - 1, bound - tallies[sink]) // 2
    margin = jnp.where((source_of == ranking[0]) | (sink == ranking[0]) | (tallies[sink] == 0), 0, jnp.maximum(margin, 0))
    passed = jax.random.randint(jax.random.fold_in(own, 4), (amount // 2,), 0, 1 << 20) % (margin + 1)
    tallies = tallies.at[source_of].add(-passed).at[sink].add(passed)
    members = jnp.searchsorted(jnp.cumsum(tallies), jnp.arange(rows * top), side="right").astype(jnp.int32)
    listing = members.reshape(top, rows).T
    listing = listing[jax.random.permutation(jax.random.fold_in(own, 1), rows)]
    offset_by = jax.random.randint(jax.random.fold_in(own, 2), (rows, 1), 0, top)
    return jnp.take_along_axis(listing, (jnp.arange(top)[None, :] + offset_by) % top, axis=1)


def portions_of(amount, total, most, slope, full):
    portions = [(1 << 20) // math.isqrt(rank ** slope) + 1 for rank in range(1, amount + 1)]
    largest = most if full else min(most, max(-(-total // amount), total * portions[0] // sum(portions)))
    least = 1 if total - largest >= amount - 1 else 0
    given, surplus = [largest] + [least] * (amount - 1), total - largest - least * (amount - 1)
    while surplus > 0:
        free = [i for i in range(1, amount) if given[i] < largest] or [i for i in range(1, amount) if given[i] < most]
        pool, left = sum([portions[i] for i in free]), surplus
        for i in free:
            extra = min(most - given[i], max(1, left * portions[i] // pool), surplus)
            given[i] = given[i] + extra
            surplus = surplus - extra
    return np.array(given)


def noise(rng, extent, scale, bound, shards=(), held_as=jnp.bfloat16):
    values = scale * jax.random.normal(rng, extent, jnp.float32)
    if shards:
        values = values * block_levels(rng, extent, shards, -0.22, 0.18)
    return jnp.clip(values, -bound, bound).astype(held_as)


def setup_inputs(seed: int = 0) -> dict:
    key_of = jax.random.split(jax.random.key(seed), 7)
    tokens = noise(key_of[0], (TOKENS, D), 1.0, 6.0, ((0, 1024),))
    upstream = noise(key_of[1], (TOKENS, D), 1.0, 6.0, ((0, 1024),))
    expert_ids_keys = jax.random.split(jax.random.fold_in(key_of[2], 1), TOKENS // TOK_DEV)
    expert_ids_turns = jax.random.permutation(jax.random.fold_in(key_of[2], 3), TOKENS // TOK_DEV)
    expert_ids = jax.vmap(lambda own, number: shared_out(jax.random.fold_in(key_of[2], 2), own, number, TOK_DEV, EXPERTS, TOP, MOST, 2))(expert_ids_keys, expert_ids_turns).reshape((TOKENS, TOP))
    gate_weights = jnp.clip(0.049804688 + 0.4501953 * jax.random.uniform(key_of[3], (TOKENS, TOP), jnp.float32) ** block_levels(key_of[3], (TOKENS, TOP), ((0, 1024),), -0.2, 0.2), 0.049804688, 0.5).astype(jnp.bfloat16)
    w_up = noise(key_of[4], (FLIGHTS, D, F), D ** -0.5, 0.125, ((0, 16),))
    w_down = noise(key_of[5], (FLIGHTS, F, D), F ** -0.5, 0.21875, ((0, 16),))
    return dict(tokens=tokens, upstream=upstream, expert_ids=expert_ids, gate_weights=gate_weights, w_up=w_up, w_down=w_down)


def reference(tokens, upstream, expert_ids, gate_weights, w_up, w_down):
    flat_ids = expert_ids.reshape(-1)
    flat_gates = gate_weights.reshape(-1)
    live = (flat_ids % EXP_DEV) == 0
    limit = N_DP * N_EXPERT * MOST

    def one_expert(index):
        hit = live & ((flat_ids // EXP_DEV) == index)
        places = jnp.nonzero(hit, size=limit, fill_value=0)[0].astype(jnp.int32)
        valid = jnp.arange(limit) < jnp.sum(hit.astype(jnp.int32))
        owners = (places // TOP).astype(jnp.int32)
        rows_x = tokens[owners]
        rows_dy = upstream[owners]
        rows_gate = jnp.where(valid, flat_gates[places].astype(jnp.float32), 0.0)
        up_mat = w_up[index]
        down_mat = w_down[index]
        act = jnp.dot(rows_x, up_mat, preferred_element_type=jnp.float32)
        sig = jax.nn.sigmoid(act)
        hidden = (act * sig).astype(jnp.bfloat16)
        expert_out = jnp.dot(hidden, down_mat, preferred_element_type=jnp.float32)
        gate_term = jnp.sum(rows_dy.astype(jnp.float32) * expert_out, axis=1)
        gate_term = jnp.where(valid, gate_term, 0.0)
        router_col = jnp.sum(gate_term[:, None] * rows_x.astype(jnp.float32), axis=0)
        scaled = (rows_gate[:, None] * rows_dy.astype(jnp.float32)).astype(jnp.bfloat16)
        back = lax.dot_general(scaled, down_mat, (((1,), (1,)), ((), ())), preferred_element_type=jnp.float32)
        act_grad = (back * sig * (1.0 + act * (1.0 - sig))).astype(jnp.bfloat16)
        route_grad = lax.dot_general(act_grad, up_mat, (((1,), (1,)), ((), ())), preferred_element_type=jnp.float32).astype(jnp.bfloat16)
        return route_grad, gate_term, router_col, places, valid

    route_grad, gate_term, router_cols, places, valid = lax.map(one_expert, jnp.arange(N_EXPERT))
    owners = (places // TOP).astype(jnp.int32).reshape(-1)
    terms = jnp.where(valid.reshape(-1)[:, None], route_grad.reshape(-1, D).astype(jnp.float32), 0.0)
    token_grads = jnp.zeros((TOKENS, D), jnp.float32).at[owners].add(terms).astype(jnp.bfloat16)
    gate_vals = gate_term.astype(jnp.bfloat16).astype(jnp.float32)
    gate_flat = jnp.zeros((TOKENS * TOP,), jnp.float32).at[places.reshape(-1)].add(jnp.where(valid, gate_vals, 0.0).reshape(-1))
    gate_grads = gate_flat.reshape(TOKENS, TOP).astype(jnp.bfloat16)
    router_grads = router_cols / jnp.float32(COLUMN_TOK)
    return token_grads, gate_grads, router_grads
```

```python
import jax
import jax.numpy as jnp
from jax import lax
from jax.sharding import PartitionSpec as P

EXP_DEV = 8


def forward_part(rows_x, up_mat, down_mat):
    act = jnp.dot(rows_x, up_mat, preferred_element_type=jnp.float32)
    sig = jax.nn.sigmoid(act)
    hidden = (act * sig).astype(jnp.bfloat16)
    expert_out = jnp.dot(hidden, down_mat, preferred_element_type=jnp.float32)
    return (act, sig, expert_out)


def scale_part(expert_out, rows_dy, rows_gate):
    dy_wide = rows_dy.astype(jnp.float32)
    gate_term = jnp.sum(dy_wide * expert_out, axis=1)
    scaled = (rows_gate.astype(jnp.float32)[:, None] * dy_wide).astype(jnp.bfloat16)
    return (gate_term, scaled)


def input_part(act, sig, scaled, up_mat, down_mat):
    back = lax.dot_general(
        scaled, down_mat, (((1,), (1,)), ((), ())), preferred_element_type=jnp.float32
    )
    act_grad = (back * sig * (1.0 + act * (1.0 - sig))).astype(jnp.bfloat16)
    return lax.dot_general(
        act_grad, up_mat, (((1,), (1,)), ((), ())), preferred_element_type=jnp.float32
    ).astype(jnp.bfloat16)


def router_total(local_col, column_tok):
    n = lax.axis_size("dp")
    acc = local_col
    d = 1
    while d < n:
        perm = [(i, i ^ d) for i in range(n)]
        acc = acc + lax.ppermute(acc, "dp", perm)
        d *= 2
    return acc / jnp.float32(column_tok)


def body(tokens, upstream, expert_ids, gate_weights, w_up, w_down):
    owners_count = lax.axis_size("expert")
    experts = EXP_DEV * owners_count
    tok_count = tokens.shape[0]
    top = expert_ids.shape[1]
    width = tokens.shape[1]
    column_tok = tok_count * lax.axis_size("dp")
    most = tok_count * top // experts + tok_count * top // (4 * experts)
    slots_all = owners_count * most
    up_mat = w_up[0]
    down_mat = w_down[0]
    flat_ids = expert_ids.reshape(-1)
    live = flat_ids % EXP_DEV == 0
    target = flat_ids // EXP_DEV
    onehot = ((target[:, None] == jnp.arange(owners_count)[None, :]) & live[:, None]).astype(
        jnp.int32
    )
    before = jnp.cumsum(onehot, axis=0) - onehot
    slot = jnp.sum(before * onehot, axis=1)
    place = jnp.where(live, target * most + slot, -1)
    route_pick = place[None, :] == jnp.arange(slots_all)[:, None]
    token_pick = jnp.any(route_pick.reshape(slots_all, tok_count, top), axis=2).astype(jnp.bfloat16)
    route_table = route_pick.astype(jnp.bfloat16)
    send_x = (
        jnp.dot(token_pick, tokens, preferred_element_type=jnp.float32)
        .astype(jnp.bfloat16)
        .reshape(owners_count, most, width)
    )
    send_dy = (
        jnp.dot(token_pick, upstream, preferred_element_type=jnp.float32)
        .astype(jnp.bfloat16)
        .reshape(owners_count, most, width)
    )
    send_gate = (
        jnp.dot(route_table, gate_weights.reshape(-1), preferred_element_type=jnp.float32)
        .astype(jnp.bfloat16)
        .reshape(owners_count, most)
    )
    rows_x = lax.all_to_all(send_x, "expert", split_axis=0, concat_axis=0, tiled=True)
    rows_dy = lax.all_to_all(send_dy, "expert", split_axis=0, concat_axis=0, tiled=True)
    rows_gate = lax.all_to_all(send_gate, "expert", split_axis=0, concat_axis=0, tiled=True)
    groups = rows_gate.shape[0]
    count = rows_gate.shape[1]
    flat_x = rows_x.reshape(groups * count, width)
    act, sig, expert_out = forward_part(flat_x, up_mat, down_mat)
    gate_term, scaled = scale_part(
        expert_out, rows_dy.reshape(groups * count, width), rows_gate.reshape(-1)
    )
    route_grad = input_part(act, sig, scaled, up_mat, down_mat)
    weighted = (gate_term[:, None] * flat_x.astype(jnp.float32)).reshape(groups, count, width)
    back_rows = lax.all_to_all(
        route_grad.reshape(groups, count, width), "expert", split_axis=0, concat_axis=0, tiled=True
    )
    back_gate = lax.all_to_all(
        gate_term.astype(jnp.bfloat16).reshape(groups, count),
        "expert",
        split_axis=0,
        concat_axis=0,
        tiled=True,
    )
    back_rows, back_gate, weighted_all = (back_rows, back_gate, weighted)
    router_grads = router_total(jnp.sum(weighted_all, axis=(0, 1)), column_tok)
    token_grads = lax.dot_general(
        token_pick,
        back_rows.reshape(slots_all, width),
        (((0,), (0,)), ((), ())),
        preferred_element_type=jnp.float32,
    ).astype(jnp.bfloat16)
    gate_flat = lax.dot_general(
        route_table,
        back_gate.reshape(slots_all),
        (((0,), (0,)), ((), ())),
        preferred_element_type=jnp.float32,
    )
    gate_grads = gate_flat.reshape(tok_count, top).astype(jnp.bfloat16)
    return (token_grads, gate_grads, router_grads[None])


def solution(mesh):
    return jax.shard_map(
        body,
        mesh=mesh,
        in_specs=(
            P(("dp", "expert"), None),
            P(("dp", "expert"), None),
            P(("dp", "expert"), None),
            P(("dp", "expert"), None),
            P("expert", None, None),
            P("expert", None, None),
        ),
        out_specs=(P(("dp", "expert"), None), P(("dp", "expert"), None), P("expert", None)),
        check_vma=False,
    )
```

```python
import jax
import jax.numpy as jnp
from jax import lax
from jax.sharding import PartitionSpec as P

EXP_DEV = 8
DP_REDUCE = "a2a"


def dp_sum(local_col):
    n = lax.axis_size("dp")
    width = local_col.shape[0]
    if DP_REDUCE == "a2a":
        parts = local_col.reshape(n, width // n)
        mine = jnp.sum(lax.all_to_all(parts, "dp", 0, 0, tiled=True), axis=0)
        spread = jnp.broadcast_to(mine[None], (n, width // n))
        return lax.all_to_all(spread, "dp", 0, 0, tiled=True).reshape(width)
    acc = local_col
    d = 1
    while d < n:
        acc = acc + lax.ppermute(acc, "dp", [(i, i ^ d) for i in range(n)])
        d *= 2
    return acc


def body(tokens, upstream, expert_ids, gate_weights, w_up, w_down):
    owners = lax.axis_size("expert")
    experts = EXP_DEV * owners
    tok_count, top = expert_ids.shape
    width = tokens.shape[1]
    column_tok = tok_count * lax.axis_size("dp")
    most = tok_count * top // experts + tok_count * top // (4 * experts)
    up_mat = w_up[0]
    down_mat = w_down[0]
    live = expert_ids % EXP_DEV == 0
    target = expert_ids // EXP_DEV
    hit = (target[:, :, None] == jnp.arange(owners)[None, None, :]) & live[:, :, None]
    hit_f = hit.astype(jnp.float32)
    tok_oh = jnp.sum(hit_f, axis=1)
    lower = (jnp.arange(tok_count)[None, :] < jnp.arange(tok_count)[:, None]).astype(jnp.float32)
    before = jnp.dot(lower, tok_oh, preferred_element_type=jnp.float32)
    slot_hit = before.T[:, None, :] == jnp.arange(most, dtype=jnp.float32)[None, :, None]
    pick = (slot_hit & (tok_oh.T[:, None, :] > 0)).astype(jnp.bfloat16)
    gate_tc = jnp.sum(hit_f * gate_weights.astype(jnp.float32)[:, :, None], axis=1)
    send_x = jnp.einsum("cst,td->csd", pick, tokens, preferred_element_type=jnp.float32)
    send_dy = jnp.einsum("cst,td->csd", pick, upstream, preferred_element_type=jnp.float32)
    send_gate = jnp.einsum(
        "cst,tc->cs", pick.astype(jnp.float32), gate_tc, preferred_element_type=jnp.float32
    )
    gate_cols = jnp.broadcast_to(send_gate[:, :, None], (owners, most, 128))
    packed = jnp.concatenate([send_x, send_dy, gate_cols], axis=2).astype(jnp.bfloat16)
    recv = lax.all_to_all(packed, "expert", 0, 0, tiled=True)
    rows_x = recv[:, :, :width]
    rows_dy = recv[:, :, width : 2 * width]
    rows_gate = recv[:, :, 2 * width]
    act = jnp.einsum("gsd,df->gsf", rows_x, up_mat, preferred_element_type=jnp.float32)
    sig = jax.nn.sigmoid(act)
    hidden = (act * sig).astype(jnp.bfloat16)
    expert_out = jnp.einsum("gsf,fd->gsd", hidden, down_mat, preferred_element_type=jnp.float32)
    dy_wide = rows_dy.astype(jnp.float32)
    gate_term = jnp.sum(dy_wide * expert_out, axis=2)
    local_col = jnp.sum(gate_term[:, :, None] * rows_x.astype(jnp.float32), axis=(0, 1))
    router_grads = dp_sum(local_col) / jnp.float32(column_tok)
    scaled = (rows_gate.astype(jnp.float32)[:, :, None] * dy_wide).astype(jnp.bfloat16)
    back = jnp.einsum("gsd,fd->gsf", scaled, down_mat, preferred_element_type=jnp.float32)
    act_grad = (back * sig * (1.0 + act * (1.0 - sig))).astype(jnp.bfloat16)
    route_grad = jnp.einsum(
        "gsf,df->gsd", act_grad, up_mat, preferred_element_type=jnp.float32
    ).astype(jnp.bfloat16)
    gate_back = jnp.broadcast_to(gate_term.astype(jnp.bfloat16)[:, :, None], (owners, most, 128))
    returned = lax.all_to_all(
        jnp.concatenate([route_grad, gate_back], axis=2), "expert", 0, 0, tiled=True
    )
    back_rows = returned[:, :, :width]
    back_gate = returned[:, :, width].astype(jnp.float32)
    token_grads = jnp.einsum(
        "cst,csd->td", pick, back_rows, preferred_element_type=jnp.float32
    ).astype(jnp.bfloat16)
    gate_back_tc = jnp.einsum(
        "cst,cs->tc", pick.astype(jnp.float32), back_gate, preferred_element_type=jnp.float32
    )
    gate_grads = jnp.sum(hit_f * gate_back_tc[:, None, :], axis=2).astype(jnp.bfloat16)
    return (token_grads, gate_grads, router_grads[None])


def solution(mesh):
    return jax.shard_map(
        body,
        mesh=mesh,
        in_specs=(
            P(("dp", "expert"), None),
            P(("dp", "expert"), None),
            P(("dp", "expert"), None),
            P(("dp", "expert"), None),
            P("expert", None, None),
            P("expert", None, None),
        ),
        out_specs=(P(("dp", "expert"), None), P(("dp", "expert"), None), P("expert", None)),
        check_vma=False,
    )
```

```python
import jax
import jax.numpy as jnp
from jax import lax
from jax.sharding import PartitionSpec as P

EXP_DEV = 8
DP_REDUCE = "sc"


def dp_sum(local_col):
    n = lax.axis_size("dp")
    width = local_col.shape[0]
    if DP_REDUCE == "sc":
        b = jnp.broadcast_to(local_col, (16, width)) * (jnp.arange(16) == 0).astype(jnp.float32)[:, None]
        return jnp.sum(lax.psum(b, "dp"), axis=0)
    if DP_REDUCE == "a2a":
        parts = local_col.reshape(n, width // n)
        mine = jnp.sum(lax.all_to_all(parts, "dp", 0, 0, tiled=True), axis=0)
        spread = jnp.broadcast_to(mine[None], (n, width // n))
        return lax.all_to_all(spread, "dp", 0, 0, tiled=True).reshape(width)
    acc = local_col
    d = 1
    while d < n:
        acc = acc + lax.ppermute(acc, "dp", [(i, i ^ d) for i in range(n)])
        d *= 2
    return acc


def body(tokens, upstream, expert_ids, gate_weights, w_up, w_down):
    owners = lax.axis_size("expert")
    experts = EXP_DEV * owners
    tok_count, top = expert_ids.shape
    width = tokens.shape[1]
    column_tok = tok_count * lax.axis_size("dp")
    most = tok_count * top // experts + tok_count * top // (4 * experts)
    up_mat = w_up[0]
    down_mat = w_down[0]
    live = expert_ids % EXP_DEV == 0
    target = expert_ids // EXP_DEV
    hit = (target[:, :, None] == jnp.arange(owners)[None, None, :]) & live[:, :, None]
    hit_f = hit.astype(jnp.float32)
    tok_oh = jnp.sum(hit_f, axis=1)
    lower = (jnp.arange(tok_count)[None, :] < jnp.arange(tok_count)[:, None]).astype(jnp.float32)
    before = jnp.dot(lower, tok_oh, preferred_element_type=jnp.float32)
    slot_hit = before.T[:, None, :] == jnp.arange(most, dtype=jnp.float32)[None, :, None]
    pick = (slot_hit & (tok_oh.T[:, None, :] > 0)).astype(jnp.bfloat16)
    gate_tc = jnp.sum(hit_f * gate_weights.astype(jnp.float32)[:, :, None], axis=1)
    send_x = jnp.einsum("cst,td->csd", pick, tokens, preferred_element_type=jnp.float32)
    send_dy = jnp.einsum("cst,td->csd", pick, upstream, preferred_element_type=jnp.float32)
    send_gate = jnp.einsum(
        "cst,tc->cs", pick.astype(jnp.float32), gate_tc, preferred_element_type=jnp.float32
    )
    gate_cols = jnp.broadcast_to(send_gate[:, :, None], (owners, most, 128))
    packed = jnp.concatenate([send_x, send_dy, gate_cols], axis=2).astype(jnp.bfloat16)
    recv = lax.all_to_all(packed, "expert", 0, 0, tiled=True)
    rows_x = recv[:, :, :width]
    rows_dy = recv[:, :, width : 2 * width]
    rows_gate = recv[:, :, 2 * width]
    act = jnp.einsum("gsd,df->gsf", rows_x, up_mat, preferred_element_type=jnp.float32)
    sig = jax.nn.sigmoid(act)
    hidden = (act * sig).astype(jnp.bfloat16)
    expert_out = jnp.einsum("gsf,fd->gsd", hidden, down_mat, preferred_element_type=jnp.float32)
    dy_wide = rows_dy.astype(jnp.float32)
    gate_term = jnp.sum(dy_wide * expert_out, axis=2)
    local_col = jnp.sum(gate_term[:, :, None] * rows_x.astype(jnp.float32), axis=(0, 1))
    router_grads = dp_sum(local_col) / jnp.float32(column_tok)
    scaled = (rows_gate.astype(jnp.float32)[:, :, None] * dy_wide).astype(jnp.bfloat16)
    back = jnp.einsum("gsd,fd->gsf", scaled, down_mat, preferred_element_type=jnp.float32)
    act_grad = (back * sig * (1.0 + act * (1.0 - sig))).astype(jnp.bfloat16)
    route_grad = jnp.einsum(
        "gsf,df->gsd", act_grad, up_mat, preferred_element_type=jnp.float32
    ).astype(jnp.bfloat16)
    gate_back = jnp.broadcast_to(gate_term.astype(jnp.bfloat16)[:, :, None], (owners, most, 128))
    returned = lax.all_to_all(
        jnp.concatenate([route_grad, gate_back], axis=2), "expert", 0, 0, tiled=True
    )
    back_rows = returned[:, :, :width]
    back_gate = returned[:, :, width].astype(jnp.float32)
    token_grads = jnp.einsum(
        "cst,csd->td", pick, back_rows, preferred_element_type=jnp.float32
    ).astype(jnp.bfloat16)
    gate_back_tc = jnp.einsum(
        "cst,cs->tc", pick.astype(jnp.float32), back_gate, preferred_element_type=jnp.float32
    )
    gate_grads = jnp.sum(hit_f * gate_back_tc[:, None, :], axis=2).astype(jnp.bfloat16)
    return (token_grads, gate_grads, router_grads[None])


def solution(mesh):
    return jax.shard_map(
        body,
        mesh=mesh,
        in_specs=(
            P(("dp", "expert"), None),
            P(("dp", "expert"), None),
            P(("dp", "expert"), None),
            P(("dp", "expert"), None),
            P("expert", None, None),
            P("expert", None, None),
        ),
        out_specs=(P(("dp", "expert"), None), P(("dp", "expert"), None), P("expert", None)),
        check_vma=False,
    )
```

```python
import jax
import jax.numpy as jnp
from jax import lax
from jax.sharding import PartitionSpec as P

EXP_DEV = 8


def dp_sum(local_col):
    n = lax.axis_size("dp")
    me = lax.axis_index("dp")
    near = 8
    far = n // near
    pos = jnp.arange(near)
    got = [local_col] + [
        lax.ppermute(local_col, "dp", [(i, i ^ j) for i in range(n)]) for j in range(1, near)
    ]
    group = jnp.sum(jnp.stack(got)[pos ^ (me % near)], axis=0)
    got = [group] + [
        lax.ppermute(group, "dp", [(i, (i + near * m) % n) for i in range(n)])
        for m in range(1, far)
    ]
    order = (me // near - jnp.arange(far)) % far
    return jnp.sum(jnp.stack(got)[order], axis=0)


def body(tokens, upstream, expert_ids, gate_weights, w_up, w_down):
    owners = lax.axis_size("expert")
    experts = EXP_DEV * owners
    tok_count, top = expert_ids.shape
    width = tokens.shape[1]
    column_tok = tok_count * lax.axis_size("dp")
    most = tok_count * top // experts + tok_count * top // (4 * experts)
    up_mat = w_up[0]
    down_mat = w_down[0]
    live = expert_ids % EXP_DEV == 0
    target = expert_ids // EXP_DEV
    hit = (target[:, :, None] == jnp.arange(owners)[None, None, :]) & live[:, :, None]
    hit_f = hit.astype(jnp.float32)
    tok_oh = jnp.sum(hit_f, axis=1)
    lower = (jnp.arange(tok_count)[None, :] < jnp.arange(tok_count)[:, None]).astype(jnp.float32)
    before = jnp.dot(lower, tok_oh, preferred_element_type=jnp.float32)
    slot_hit = before.T[:, None, :] == jnp.arange(most, dtype=jnp.float32)[None, :, None]
    pick = (slot_hit & (tok_oh.T[:, None, :] > 0)).astype(jnp.bfloat16)
    gate_tc = jnp.sum(hit_f * gate_weights.astype(jnp.float32)[:, :, None], axis=1)
    send_x = jnp.einsum("cst,td->csd", pick, tokens, preferred_element_type=jnp.float32)
    send_dy = jnp.einsum("cst,td->csd", pick, upstream, preferred_element_type=jnp.float32)
    send_gate = jnp.einsum(
        "cst,tc->cs", pick.astype(jnp.float32), gate_tc, preferred_element_type=jnp.float32
    )
    gate_cols = jnp.broadcast_to(send_gate[:, :, None], (owners, most, 128))
    packed = jnp.concatenate([send_x, send_dy, gate_cols], axis=2).astype(jnp.bfloat16)
    recv = lax.all_to_all(packed, "expert", 0, 0, tiled=True)
    rows_x = recv[:, :, :width]
    rows_dy = recv[:, :, width : 2 * width]
    rows_gate = recv[:, :, 2 * width]
    act = jnp.einsum("gsd,df->gsf", rows_x, up_mat, preferred_element_type=jnp.float32)
    sig = jax.nn.sigmoid(act)
    hidden = (act * sig).astype(jnp.bfloat16)
    expert_out = jnp.einsum("gsf,fd->gsd", hidden, down_mat, preferred_element_type=jnp.float32)
    dy_wide = rows_dy.astype(jnp.float32)
    gate_term = jnp.sum(dy_wide * expert_out, axis=2)
    local_col = jnp.sum(gate_term[:, :, None] * rows_x.astype(jnp.float32), axis=(0, 1))
    router_grads = dp_sum(local_col) / jnp.float32(column_tok)
    scaled = (rows_gate.astype(jnp.float32)[:, :, None] * dy_wide).astype(jnp.bfloat16)
    back = jnp.einsum("gsd,fd->gsf", scaled, down_mat, preferred_element_type=jnp.float32)
    act_grad = (back * sig * (1.0 + act * (1.0 - sig))).astype(jnp.bfloat16)
    route_grad = jnp.einsum(
        "gsf,df->gsd", act_grad, up_mat, preferred_element_type=jnp.float32
    ).astype(jnp.bfloat16)
    gate_back = jnp.broadcast_to(gate_term.astype(jnp.bfloat16)[:, :, None], (owners, most, 128))
    returned = lax.all_to_all(
        jnp.concatenate([route_grad, gate_back], axis=2), "expert", 0, 0, tiled=True
    )
    back_rows = returned[:, :, :width]
    back_gate = returned[:, :, width].astype(jnp.float32)
    token_grads = jnp.einsum(
        "cst,csd->td", pick, back_rows, preferred_element_type=jnp.float32
    ).astype(jnp.bfloat16)
    gate_back_tc = jnp.einsum(
        "cst,cs->tc", pick.astype(jnp.float32), back_gate, preferred_element_type=jnp.float32
    )
    gate_grads = jnp.sum(hit_f * gate_back_tc[:, None, :], axis=2).astype(jnp.bfloat16)
    return (token_grads, gate_grads, router_grads[None])


def solution(mesh):
    return jax.shard_map(
        body,
        mesh=mesh,
        in_specs=(
            P(("dp", "expert"), None),
            P(("dp", "expert"), None),
            P(("dp", "expert"), None),
            P(("dp", "expert"), None),
            P("expert", None, None),
            P("expert", None, None),
        ),
        out_specs=(P(("dp", "expert"), None), P(("dp", "expert"), None), P("expert", None)),
        check_vma=False,
    )
```

```python
import jax
import jax.numpy as jnp
from jax import lax
from jax.sharding import Mesh, PartitionSpec as P

EXP_DEV = 8


def dp_sum(local_col):
    return lax.psum(lax.psum(lax.psum(local_col, "core"), "near"), "far")


def body(tokens, upstream, expert_ids, gate_weights, w_up, w_down):
    owners = lax.axis_size("expert")
    experts = EXP_DEV * owners
    tok_count, top = expert_ids.shape
    width = tokens.shape[1]
    column_tok = tok_count * lax.axis_size(("far", "near", "core"))
    most = tok_count * top // experts + tok_count * top // (4 * experts)
    up_mat = w_up[0]
    down_mat = w_down[0]
    live = expert_ids % EXP_DEV == 0
    target = expert_ids // EXP_DEV
    hit = (target[:, :, None] == jnp.arange(owners)[None, None, :]) & live[:, :, None]
    hit_f = hit.astype(jnp.float32)
    tok_oh = jnp.sum(hit_f, axis=1)
    lower = (jnp.arange(tok_count)[None, :] < jnp.arange(tok_count)[:, None]).astype(jnp.float32)
    before = jnp.dot(lower, tok_oh, preferred_element_type=jnp.float32)
    slot_hit = before.T[:, None, :] == jnp.arange(most, dtype=jnp.float32)[None, :, None]
    pick = (slot_hit & (tok_oh.T[:, None, :] > 0)).astype(jnp.bfloat16)
    gate_tc = jnp.sum(hit_f * gate_weights.astype(jnp.float32)[:, :, None], axis=1)
    send_x = jnp.einsum("cst,td->csd", pick, tokens, preferred_element_type=jnp.float32)
    send_dy = jnp.einsum("cst,td->csd", pick, upstream, preferred_element_type=jnp.float32)
    send_gate = jnp.einsum(
        "cst,tc->cs", pick.astype(jnp.float32), gate_tc, preferred_element_type=jnp.float32
    )
    gate_cols = jnp.broadcast_to(send_gate[:, :, None], (owners, most, 128))
    packed = jnp.concatenate([send_x, send_dy, gate_cols], axis=2).astype(jnp.bfloat16)
    recv = lax.all_to_all(packed, "expert", 0, 0, tiled=True)
    rows_x = recv[:, :, :width]
    rows_dy = recv[:, :, width : 2 * width]
    rows_gate = recv[:, :, 2 * width]
    act = jnp.einsum("gsd,df->gsf", rows_x, up_mat, preferred_element_type=jnp.float32)
    sig = jax.nn.sigmoid(act)
    hidden = (act * sig).astype(jnp.bfloat16)
    expert_out = jnp.einsum("gsf,fd->gsd", hidden, down_mat, preferred_element_type=jnp.float32)
    dy_wide = rows_dy.astype(jnp.float32)
    gate_term = jnp.sum(dy_wide * expert_out, axis=2)
    local_col = jnp.sum(gate_term[:, :, None] * rows_x.astype(jnp.float32), axis=(0, 1))
    router_grads = dp_sum(local_col) / jnp.float32(column_tok)
    scaled = (rows_gate.astype(jnp.float32)[:, :, None] * dy_wide).astype(jnp.bfloat16)
    back = jnp.einsum("gsd,fd->gsf", scaled, down_mat, preferred_element_type=jnp.float32)
    act_grad = (back * sig * (1.0 + act * (1.0 - sig))).astype(jnp.bfloat16)
    route_grad = jnp.einsum(
        "gsf,df->gsd", act_grad, up_mat, preferred_element_type=jnp.float32
    ).astype(jnp.bfloat16)
    gate_back = jnp.broadcast_to(gate_term.astype(jnp.bfloat16)[:, :, None], (owners, most, 128))
    returned = lax.all_to_all(
        jnp.concatenate([route_grad, gate_back], axis=2), "expert", 0, 0, tiled=True
    )
    back_rows = returned[:, :, :width]
    back_gate = returned[:, :, width].astype(jnp.float32)
    token_grads = jnp.einsum(
        "cst,csd->td", pick, back_rows, preferred_element_type=jnp.float32
    ).astype(jnp.bfloat16)
    gate_back_tc = jnp.einsum(
        "cst,cs->tc", pick.astype(jnp.float32), back_gate, preferred_element_type=jnp.float32
    )
    gate_grads = jnp.sum(hit_f * gate_back_tc[:, None, :], axis=2).astype(jnp.bfloat16)
    return (token_grads, gate_grads, router_grads[None])


def solution(mesh):
    n_dp = mesh.shape["dp"]
    rows = ("far", "near", "core", "expert")
    split = Mesh(
        mesh.devices.reshape(n_dp // 8, 4, 2, mesh.shape["expert"]), rows
    )
    return jax.shard_map(
        body,
        mesh=split,
        in_specs=(
            P(rows, None),
            P(rows, None),
            P(rows, None),
            P(rows, None),
            P("expert", None, None),
            P("expert", None, None),
        ),
        out_specs=(P(rows, None), P(rows, None), P("expert", None)),
        check_vma=False,
    )
```

```python
import jax
import jax.numpy as jnp
from jax import lax
from jax.sharding import Mesh, PartitionSpec as P

EXP_DEV = 8


def dp_sum(local_col):
    return lax.psum(lax.psum(lax.psum(local_col, "core"), "near"), "far")


def body(tokens, upstream, expert_ids, gate_weights, w_up, w_down):
    owners = lax.axis_size("expert")
    experts = EXP_DEV * owners
    tok_count, top = expert_ids.shape
    width = tokens.shape[1]
    column_tok = tok_count * lax.axis_size(("far", "near", "core"))
    most = tok_count * top // experts + tok_count * top // (4 * experts)
    up_mat = w_up[0]
    down_mat = w_down[0]
    live = expert_ids % EXP_DEV == 0
    target = expert_ids // EXP_DEV
    hit = (target[:, :, None] == jnp.arange(owners)[None, None, :]) & live[:, :, None]
    hit_f = hit.astype(jnp.float32)
    tok_oh = jnp.sum(hit_f, axis=1)
    lower = (jnp.arange(tok_count)[None, :] < jnp.arange(tok_count)[:, None]).astype(jnp.float32)
    before = jnp.dot(lower, tok_oh, preferred_element_type=jnp.float32)
    slot_hit = before.T[:, None, :] == jnp.arange(most, dtype=jnp.float32)[None, :, None]
    pick = (slot_hit & (tok_oh.T[:, None, :] > 0)).astype(jnp.bfloat16)
    gate_tc = jnp.sum(hit_f * gate_weights.astype(jnp.float32)[:, :, None], axis=1)
    send_x = jnp.einsum("cst,td->csd", pick, tokens, preferred_element_type=jnp.float32)
    send_dy = jnp.einsum("cst,td->csd", pick, upstream, preferred_element_type=jnp.float32)
    send_gate = jnp.einsum(
        "cst,tc->cs", pick.astype(jnp.float32), gate_tc, preferred_element_type=jnp.float32
    )
    gate_cols = jnp.broadcast_to(send_gate[:, :, None], (owners, most, 128))
    packed = jnp.concatenate([send_dy, gate_cols], axis=2).astype(jnp.bfloat16)
    rows_x = lax.all_to_all(send_x.astype(jnp.bfloat16), "expert", 0, 0, tiled=True)
    recv = lax.all_to_all(packed, "expert", 0, 0, tiled=True)
    rows_dy = recv[:, :, :width]
    rows_gate = recv[:, :, width]
    act = jnp.einsum("gsd,df->gsf", rows_x, up_mat, preferred_element_type=jnp.float32)
    sig = jax.nn.sigmoid(act)
    hidden = (act * sig).astype(jnp.bfloat16)
    expert_out = jnp.einsum("gsf,fd->gsd", hidden, down_mat, preferred_element_type=jnp.float32)
    dy_wide = rows_dy.astype(jnp.float32)
    gate_term = jnp.sum(dy_wide * expert_out, axis=2)
    local_col = jnp.sum(gate_term[:, :, None] * rows_x.astype(jnp.float32), axis=(0, 1))
    router_grads = dp_sum(local_col) / jnp.float32(column_tok)
    scaled = (rows_gate.astype(jnp.float32)[:, :, None] * dy_wide).astype(jnp.bfloat16)
    back = jnp.einsum("gsd,fd->gsf", scaled, down_mat, preferred_element_type=jnp.float32)
    act_grad = (back * sig * (1.0 + act * (1.0 - sig))).astype(jnp.bfloat16)
    route_grad = jnp.einsum(
        "gsf,df->gsd", act_grad, up_mat, preferred_element_type=jnp.float32
    ).astype(jnp.bfloat16)
    gate_back = jnp.broadcast_to(gate_term.astype(jnp.bfloat16)[:, :, None], (owners, most, 128))
    returned = lax.all_to_all(
        jnp.concatenate([route_grad, gate_back], axis=2), "expert", 0, 0, tiled=True
    )
    back_rows = returned[:, :, :width]
    back_gate = returned[:, :, width].astype(jnp.float32)
    token_grads = jnp.einsum(
        "cst,csd->td", pick, back_rows, preferred_element_type=jnp.float32
    ).astype(jnp.bfloat16)
    gate_back_tc = jnp.einsum(
        "cst,cs->tc", pick.astype(jnp.float32), back_gate, preferred_element_type=jnp.float32
    )
    gate_grads = jnp.sum(hit_f * gate_back_tc[:, None, :], axis=2).astype(jnp.bfloat16)
    return (token_grads, gate_grads, router_grads[None])


def solution(mesh):
    n_dp = mesh.shape["dp"]
    rows = ("far", "near", "core", "expert")
    split = Mesh(
        mesh.devices.reshape(n_dp // 8, 4, 2, mesh.shape["expert"]), rows
    )
    return jax.shard_map(
        body,
        mesh=split,
        in_specs=(
            P(rows, None),
            P(rows, None),
            P(rows, None),
            P(rows, None),
            P("expert", None, None),
            P("expert", None, None),
        ),
        out_specs=(P(rows, None), P(rows, None), P("expert", None)),
        check_vma=False,
    )
```

```python
import jax
import jax.numpy as jnp
from jax import lax
from jax.sharding import Mesh, PartitionSpec as P

EXP_DEV = 8


def dp_sum(local_col):
    return lax.psum(lax.psum(lax.psum(local_col, "core"), "near"), "far")


def body(tokens, upstream, expert_ids, gate_weights, w_up, w_down):
    owners = lax.axis_size("expert")
    experts = EXP_DEV * owners
    tok_count, top = expert_ids.shape
    width = tokens.shape[1]
    column_tok = tok_count * lax.axis_size(("far", "near", "core"))
    most = tok_count * top // experts + tok_count * top // (4 * experts)
    slots = -(-most // 8) * 8
    rows_all = owners * slots
    up_mat = w_up[0]
    down_mat = w_down[0]
    live = expert_ids % EXP_DEV == 0
    target = expert_ids // EXP_DEV
    hit = (target[:, :, None] == jnp.arange(owners)[None, None, :]) & live[:, :, None]
    hit_f = hit.astype(jnp.float32)
    tok_oh = jnp.sum(hit_f, axis=1)
    lower = (jnp.arange(tok_count)[None, :] < jnp.arange(tok_count)[:, None]).astype(jnp.float32)
    before = jnp.dot(lower, tok_oh, preferred_element_type=jnp.float32)
    slot_hit = before.T[:, None, :] == jnp.arange(slots, dtype=jnp.float32)[None, :, None]
    pick3 = slot_hit & (tok_oh.T[:, None, :] > 0)
    pick = pick3.reshape(rows_all, tok_count).astype(jnp.bfloat16)
    gate_tc = jnp.sum(hit_f * gate_weights.astype(jnp.float32)[:, :, None], axis=1)
    send_x = jnp.dot(pick, tokens, preferred_element_type=jnp.float32)
    send_dy = jnp.dot(pick, upstream, preferred_element_type=jnp.float32)
    send_gate = jnp.einsum(
        "cst,tc->cs", pick3.astype(jnp.float32), gate_tc, preferred_element_type=jnp.float32
    ).reshape(rows_all)
    gate_cols = jnp.broadcast_to(send_gate[:, None], (rows_all, 128))
    packed = jnp.concatenate([send_x, send_dy, gate_cols], axis=1).astype(jnp.bfloat16)
    recv = lax.all_to_all(
        packed.reshape(owners, slots, -1), "expert", 0, 0, tiled=True
    ).reshape(rows_all, -1)
    rows_x = recv[:, :width]
    rows_dy = recv[:, width : 2 * width]
    rows_gate = recv[:, 2 * width]
    act = jnp.dot(rows_x, up_mat, preferred_element_type=jnp.float32)
    sig = jax.nn.sigmoid(act)
    hidden = (act * sig).astype(jnp.bfloat16)
    expert_out = jnp.dot(hidden, down_mat, preferred_element_type=jnp.float32)
    dy_wide = rows_dy.astype(jnp.float32)
    gate_term = jnp.sum(dy_wide * expert_out, axis=1)
    local_col = jnp.sum(gate_term[:, None] * rows_x.astype(jnp.float32), axis=0)
    router_grads = dp_sum(local_col) / jnp.float32(column_tok)
    scaled = (rows_gate.astype(jnp.float32)[:, None] * dy_wide).astype(jnp.bfloat16)
    back = lax.dot_general(
        scaled, down_mat, (((1,), (1,)), ((), ())), preferred_element_type=jnp.float32
    )
    act_grad = (back * sig * (1.0 + act * (1.0 - sig))).astype(jnp.bfloat16)
    route_grad = lax.dot_general(
        act_grad, up_mat, (((1,), (1,)), ((), ())), preferred_element_type=jnp.float32
    ).astype(jnp.bfloat16)
    gate_back = jnp.broadcast_to(gate_term.astype(jnp.bfloat16)[:, None], (rows_all, 128))
    returned = lax.all_to_all(
        jnp.concatenate([route_grad, gate_back], axis=1).reshape(owners, slots, -1),
        "expert",
        0,
        0,
        tiled=True,
    ).reshape(rows_all, -1)
    back_rows = returned[:, :width]
    back_gate = returned[:, width].astype(jnp.float32).reshape(owners, slots)
    token_grads = lax.dot_general(
        pick, back_rows, (((0,), (0,)), ((), ())), preferred_element_type=jnp.float32
    ).astype(jnp.bfloat16)
    gate_back_tc = jnp.einsum(
        "cst,cs->tc", pick3.astype(jnp.float32), back_gate, preferred_element_type=jnp.float32
    )
    gate_grads = jnp.sum(hit_f * gate_back_tc[:, None, :], axis=2).astype(jnp.bfloat16)
    return (token_grads, gate_grads, router_grads[None])


def solution(mesh):
    n_dp = mesh.shape["dp"]
    rows = ("far", "near", "core", "expert")
    split = Mesh(
        mesh.devices.reshape(n_dp // 8, 4, 2, mesh.shape["expert"]), rows
    )
    return jax.shard_map(
        body,
        mesh=split,
        in_specs=(
            P(rows, None),
            P(rows, None),
            P(rows, None),
            P(rows, None),
            P("expert", None, None),
            P("expert", None, None),
        ),
        out_specs=(P(rows, None), P(rows, None), P("expert", None)),
        check_vma=False,
    )
```

```python
import jax
import jax.numpy as jnp
from jax import lax
from jax.sharding import Mesh, PartitionSpec as P

EXP_DEV = 8


def dp_sum(local_col):
    return lax.psum(lax.psum(lax.psum(local_col, "core"), "near"), "far")


def body(tokens, upstream, expert_ids, gate_weights, w_up, w_down):
    owners = lax.axis_size("expert")
    experts = EXP_DEV * owners
    tok_count, top = expert_ids.shape
    width = tokens.shape[1]
    column_tok = tok_count * lax.axis_size(("far", "near", "core"))
    most = tok_count * top // experts + tok_count * top // (4 * experts)
    slots = -(-(most + 1) // 8) * 8
    rows_all = owners * slots
    up_mat = w_up[0]
    down_mat = w_down[0]
    live = expert_ids % EXP_DEV == 0
    target = expert_ids // EXP_DEV
    hit = (target[:, :, None] == jnp.arange(owners)[None, None, :]) & live[:, :, None]
    hit_f = hit.astype(jnp.float32)
    tok_oh = jnp.sum(hit_f, axis=1)
    lower = (jnp.arange(tok_count)[None, :] < jnp.arange(tok_count)[:, None]).astype(jnp.float32)
    before = jnp.dot(lower, tok_oh, preferred_element_type=jnp.float32)
    slot_hit = before.T[:, None, :] == jnp.arange(slots, dtype=jnp.float32)[None, :, None]
    pick3 = slot_hit & (tok_oh.T[:, None, :] > 0)
    pick = pick3.reshape(rows_all, tok_count).astype(jnp.bfloat16)
    gate_tc = jnp.sum(hit_f * gate_weights.astype(jnp.float32)[:, :, None], axis=1)
    send_x = jnp.dot(pick, tokens, preferred_element_type=jnp.float32)
    send_dy = jnp.dot(pick, upstream, preferred_element_type=jnp.float32)
    send_gate = jnp.einsum(
        "cst,tc->cs", pick3.astype(jnp.float32), gate_tc, preferred_element_type=jnp.float32
    ).reshape(rows_all)
    gate_rows = jnp.pad(
        send_gate.reshape(owners, 1, slots), ((0, 0), (slots - 1, 0), (0, width - slots))
    ).reshape(rows_all, width)
    packed = jnp.concatenate([send_x, send_dy + gate_rows], axis=1).astype(jnp.bfloat16)
    recv = lax.all_to_all(
        packed.reshape(owners, slots, -1), "expert", 0, 0, tiled=True
    ).reshape(rows_all, -1)
    rows_x = recv[:, :width]
    rows_dy = recv[:, width : 2 * width]
    rows_gate = recv.reshape(owners, slots, -1)[:, slots - 1, width : width + slots].reshape(rows_all)
    act = jnp.dot(rows_x, up_mat, preferred_element_type=jnp.float32)
    sig = jax.nn.sigmoid(act)
    hidden = (act * sig).astype(jnp.bfloat16)
    expert_out = jnp.dot(hidden, down_mat, preferred_element_type=jnp.float32)
    dy_wide = rows_dy.astype(jnp.float32)
    gate_term = jnp.sum(dy_wide * expert_out, axis=1)
    local_col = jnp.sum(gate_term[:, None] * rows_x.astype(jnp.float32), axis=0)
    router_grads = dp_sum(local_col) / jnp.float32(column_tok)
    scaled = (rows_gate.astype(jnp.float32)[:, None] * dy_wide).astype(jnp.bfloat16)
    back = lax.dot_general(
        scaled, down_mat, (((1,), (1,)), ((), ())), preferred_element_type=jnp.float32
    )
    act_grad = (back * sig * (1.0 + act * (1.0 - sig))).astype(jnp.bfloat16)
    route_grad = lax.dot_general(
        act_grad, up_mat, (((1,), (1,)), ((), ())), preferred_element_type=jnp.float32
    ).astype(jnp.bfloat16)
    gate_back = jnp.pad(
        gate_term.astype(jnp.bfloat16).reshape(owners, 1, slots),
        ((0, 0), (slots - 1, 0), (0, width - slots)),
    ).reshape(rows_all, width)
    returned = lax.all_to_all(
        (route_grad + gate_back).reshape(owners, slots, -1),
        "expert",
        0,
        0,
        tiled=True,
    ).reshape(rows_all, -1)
    back_rows = returned
    back_gate = returned.reshape(owners, slots, -1)[:, slots - 1, :slots].astype(jnp.float32)
    token_grads = lax.dot_general(
        pick, back_rows, (((0,), (0,)), ((), ())), preferred_element_type=jnp.float32
    ).astype(jnp.bfloat16)
    gate_back_tc = jnp.einsum(
        "cst,cs->tc", pick3.astype(jnp.float32), back_gate, preferred_element_type=jnp.float32
    )
    gate_grads = jnp.sum(hit_f * gate_back_tc[:, None, :], axis=2).astype(jnp.bfloat16)
    return (token_grads, gate_grads, router_grads[None])


def solution(mesh):
    n_dp = mesh.shape["dp"]
    rows = ("far", "near", "core", "expert")
    split = Mesh(
        mesh.devices.reshape(n_dp // 8, 4, 2, mesh.shape["expert"]), rows
    )
    return jax.shard_map(
        body,
        mesh=split,
        in_specs=(
            P(rows, None),
            P(rows, None),
            P(rows, None),
            P(rows, None),
            P("expert", None, None),
            P("expert", None, None),
        ),
        out_specs=(P(rows, None), P(rows, None), P("expert", None)),
        check_vma=False,
    )
```

```python
import jax
import jax.numpy as jnp
from jax import lax
from jax.sharding import Mesh, PartitionSpec as P

EXP_DEV = 8


def dp_sum(local_col):
    return lax.psum(lax.psum(lax.psum(local_col, "core"), "near"), "far")


def dense_all_to_all(blocks, used):
    owners, slots, cols = blocks.shape
    flat = blocks[:, :used, :].reshape(owners, 8, used * cols // 8)
    moved = lax.all_to_all(flat, "expert", 0, 0, tiled=True).reshape(owners, used, cols)
    return jnp.pad(moved, ((0, 0), (0, slots - used), (0, 0)))


def body(tokens, upstream, expert_ids, gate_weights, w_up, w_down):
    owners = lax.axis_size("expert")
    experts = EXP_DEV * owners
    tok_count, top = expert_ids.shape
    width = tokens.shape[1]
    column_tok = tok_count * lax.axis_size(("far", "near", "core"))
    most = tok_count * top // experts + tok_count * top // (4 * experts)
    slots = -(-(most + 1) // 8) * 8
    rows_all = owners * slots
    up_mat = w_up[0]
    down_mat = w_down[0]
    live = expert_ids % EXP_DEV == 0
    target = expert_ids // EXP_DEV
    hit = (target[:, :, None] == jnp.arange(owners)[None, None, :]) & live[:, :, None]
    hit_f = hit.astype(jnp.float32)
    tok_oh = jnp.sum(hit_f, axis=1)
    lower = (jnp.arange(tok_count)[None, :] < jnp.arange(tok_count)[:, None]).astype(jnp.float32)
    before = jnp.dot(lower, tok_oh, preferred_element_type=jnp.float32)
    slot_hit = before.T[:, None, :] == jnp.arange(slots, dtype=jnp.float32)[None, :, None]
    pick3 = slot_hit & (tok_oh.T[:, None, :] > 0)
    pick = pick3.reshape(rows_all, tok_count).astype(jnp.bfloat16)
    gate_tc = jnp.sum(hit_f * gate_weights.astype(jnp.float32)[:, :, None], axis=1)
    send_x = jnp.dot(pick, tokens, preferred_element_type=jnp.float32)
    send_dy = jnp.dot(pick, upstream, preferred_element_type=jnp.float32)
    send_gate = jnp.einsum(
        "cst,tc->cs", pick3.astype(jnp.float32), gate_tc, preferred_element_type=jnp.float32
    ).reshape(rows_all)
    gate_rows = jnp.pad(
        send_gate.reshape(owners, 1, slots),
        ((0, 0), (most, slots - 1 - most), (0, width - slots)),
    ).reshape(rows_all, width)
    packed = jnp.concatenate([send_x, send_dy + gate_rows], axis=1).astype(jnp.bfloat16)
    recv = dense_all_to_all(packed.reshape(owners, slots, -1), most + 1).reshape(rows_all, -1)
    rows_x = recv[:, :width]
    rows_dy = recv[:, width : 2 * width]
    rows_gate = recv.reshape(owners, slots, -1)[:, most, width : width + slots].reshape(rows_all)
    act = jnp.dot(rows_x, up_mat, preferred_element_type=jnp.float32)
    sig = jax.nn.sigmoid(act)
    hidden = (act * sig).astype(jnp.bfloat16)
    expert_out = jnp.dot(hidden, down_mat, preferred_element_type=jnp.float32)
    dy_wide = rows_dy.astype(jnp.float32)
    gate_term = jnp.sum(dy_wide * expert_out, axis=1)
    local_col = jnp.sum(gate_term[:, None] * rows_x.astype(jnp.float32), axis=0)
    router_grads = dp_sum(local_col) / jnp.float32(column_tok)
    scaled = (rows_gate.astype(jnp.float32)[:, None] * dy_wide).astype(jnp.bfloat16)
    back = lax.dot_general(
        scaled, down_mat, (((1,), (1,)), ((), ())), preferred_element_type=jnp.float32
    )
    act_grad = (back * sig * (1.0 + act * (1.0 - sig))).astype(jnp.bfloat16)
    route_grad = lax.dot_general(
        act_grad, up_mat, (((1,), (1,)), ((), ())), preferred_element_type=jnp.float32
    ).astype(jnp.bfloat16)
    gate_back = jnp.pad(
        gate_term.astype(jnp.bfloat16).reshape(owners, 1, slots),
        ((0, 0), (slots - 1, 0), (0, width - slots)),
    ).reshape(rows_all, width)
    returned = lax.all_to_all(
        (route_grad + gate_back).reshape(owners, slots, -1),
        "expert",
        0,
        0,
        tiled=True,
    ).reshape(rows_all, -1)
    back_rows = returned
    back_gate = returned.reshape(owners, slots, -1)[:, slots - 1, :slots].astype(jnp.float32)
    token_grads = lax.dot_general(
        pick, back_rows, (((0,), (0,)), ((), ())), preferred_element_type=jnp.float32
    ).astype(jnp.bfloat16)
    gate_back_tc = jnp.einsum(
        "cst,cs->tc", pick3.astype(jnp.float32), back_gate, preferred_element_type=jnp.float32
    )
    gate_grads = jnp.sum(hit_f * gate_back_tc[:, None, :], axis=2).astype(jnp.bfloat16)
    return (token_grads, gate_grads, router_grads[None])


def solution(mesh):
    n_dp = mesh.shape["dp"]
    rows = ("far", "near", "core", "expert")
    split = Mesh(
        mesh.devices.reshape(n_dp // 8, 4, 2, mesh.shape["expert"]), rows
    )
    return jax.shard_map(
        body,
        mesh=split,
        in_specs=(
            P(rows, None),
            P(rows, None),
            P(rows, None),
            P(rows, None),
            P("expert", None, None),
            P("expert", None, None),
        ),
        out_specs=(P(rows, None), P(rows, None), P("expert", None)),
        check_vma=False,
    )
```

```python
import jax
import jax.numpy as jnp
from jax import lax
from jax.sharding import Mesh, PartitionSpec as P

EXP_DEV = 8


def dp_sum(local_col):
    return lax.psum(lax.psum(lax.psum(local_col, "far"), "near"), "core")


def body(tokens, upstream, expert_ids, gate_weights, w_up, w_down):
    owners = lax.axis_size("expert")
    experts = EXP_DEV * owners
    tok_count, top = expert_ids.shape
    width = tokens.shape[1]
    column_tok = tok_count * lax.axis_size(("far", "near", "core"))
    most = tok_count * top // experts + tok_count * top // (4 * experts)
    slots = -(-(most + 1) // 8) * 8
    rows_all = owners * slots
    up_mat = w_up[0]
    down_mat = w_down[0]
    live = expert_ids % EXP_DEV == 0
    target = expert_ids // EXP_DEV
    hit = (target[:, :, None] == jnp.arange(owners)[None, None, :]) & live[:, :, None]
    hit_f = hit.astype(jnp.float32)
    tok_oh = jnp.sum(hit_f, axis=1)
    lower = (jnp.arange(tok_count)[None, :] < jnp.arange(tok_count)[:, None]).astype(jnp.float32)
    before = jnp.dot(lower, tok_oh, preferred_element_type=jnp.float32)
    slot_hit = before.T[:, None, :] == jnp.arange(slots, dtype=jnp.float32)[None, :, None]
    pick3 = slot_hit & (tok_oh.T[:, None, :] > 0)
    pick = pick3.reshape(rows_all, tok_count).astype(jnp.bfloat16)
    gate_tc = jnp.sum(hit_f * gate_weights.astype(jnp.float32)[:, :, None], axis=1)
    send_x = jnp.dot(pick, tokens, preferred_element_type=jnp.float32)
    send_dy = jnp.dot(pick, upstream, preferred_element_type=jnp.float32)
    send_gate = jnp.einsum(
        "cst,tc->cs", pick3.astype(jnp.float32), gate_tc, preferred_element_type=jnp.float32
    ).reshape(rows_all)
    gate_rows = jnp.pad(
        send_gate.reshape(owners, 1, slots), ((0, 0), (slots - 1, 0), (0, width - slots))
    ).reshape(rows_all, width)
    packed = jnp.concatenate([send_x, send_dy + gate_rows], axis=1).astype(jnp.bfloat16)
    recv = lax.all_to_all(
        packed.reshape(owners, slots, -1), "expert", 0, 0, tiled=True
    ).reshape(rows_all, -1)
    rows_x = recv[:, :width]
    rows_dy = recv[:, width : 2 * width]
    rows_gate = recv.reshape(owners, slots, -1)[:, slots - 1, width : width + slots].reshape(rows_all)
    act = jnp.dot(rows_x, up_mat, preferred_element_type=jnp.float32)
    sig = jax.nn.sigmoid(act)
    hidden = (act * sig).astype(jnp.bfloat16)
    expert_out = jnp.dot(hidden, down_mat, preferred_element_type=jnp.float32)
    dy_wide = rows_dy.astype(jnp.float32)
    gate_term = jnp.sum(dy_wide * expert_out, axis=1)
    local_col = jnp.sum(gate_term[:, None] * rows_x.astype(jnp.float32), axis=0)
    router_grads = dp_sum(local_col) / jnp.float32(column_tok)
    scaled = (rows_gate.astype(jnp.float32)[:, None] * dy_wide).astype(jnp.bfloat16)
    back = lax.dot_general(
        scaled, down_mat, (((1,), (1,)), ((), ())), preferred_element_type=jnp.float32
    )
    act_grad = (back * sig * (1.0 + act * (1.0 - sig))).astype(jnp.bfloat16)
    route_grad = lax.dot_general(
        act_grad, up_mat, (((1,), (1,)), ((), ())), preferred_element_type=jnp.float32
    ).astype(jnp.bfloat16)
    gate_back = jnp.pad(
        gate_term.astype(jnp.bfloat16).reshape(owners, 1, slots),
        ((0, 0), (slots - 1, 0), (0, width - slots)),
    ).reshape(rows_all, width)
    returned = lax.all_to_all(
        (route_grad + gate_back).reshape(owners, slots, -1),
        "expert",
        0,
        0,
        tiled=True,
    ).reshape(rows_all, -1)
    back_rows = returned
    back_gate = returned.reshape(owners, slots, -1)[:, slots - 1, :slots].astype(jnp.float32)
    token_grads = lax.dot_general(
        pick, back_rows, (((0,), (0,)), ((), ())), preferred_element_type=jnp.float32
    ).astype(jnp.bfloat16)
    gate_back_tc = jnp.einsum(
        "cst,cs->tc", pick3.astype(jnp.float32), back_gate, preferred_element_type=jnp.float32
    )
    gate_grads = jnp.sum(hit_f * gate_back_tc[:, None, :], axis=2).astype(jnp.bfloat16)
    return (token_grads, gate_grads, router_grads[None])


def solution(mesh):
    n_dp = mesh.shape["dp"]
    rows = ("far", "near", "core", "expert")
    split = Mesh(
        mesh.devices.reshape(n_dp // 8, 4, 2, mesh.shape["expert"]), rows
    )
    return jax.shard_map(
        body,
        mesh=split,
        in_specs=(
            P(rows, None),
            P(rows, None),
            P(rows, None),
            P(rows, None),
            P("expert", None, None),
            P("expert", None, None),
        ),
        out_specs=(P(rows, None), P(rows, None), P("expert", None)),
        check_vma=False,
    )
```

```python
import jax
import jax.numpy as jnp
from jax import lax
from jax.sharding import Mesh, PartitionSpec as P

EXP_DEV = 8


def dp_sum(local_col):
    return lax.psum(lax.psum(lax.psum(lax.psum(local_col, "core"), "pair"), "quad"), "far")


def body(tokens, upstream, expert_ids, gate_weights, w_up, w_down):
    owners = lax.axis_size("expert")
    experts = EXP_DEV * owners
    tok_count, top = expert_ids.shape
    width = tokens.shape[1]
    column_tok = tok_count * lax.axis_size(("far", "quad", "pair", "core"))
    most = tok_count * top // experts + tok_count * top // (4 * experts)
    slots = -(-(most + 1) // 8) * 8
    rows_all = owners * slots
    up_mat = w_up[0]
    down_mat = w_down[0]
    live = expert_ids % EXP_DEV == 0
    target = expert_ids // EXP_DEV
    hit = (target[:, :, None] == jnp.arange(owners)[None, None, :]) & live[:, :, None]
    hit_f = hit.astype(jnp.float32)
    tok_oh = jnp.sum(hit_f, axis=1)
    lower = (jnp.arange(tok_count)[None, :] < jnp.arange(tok_count)[:, None]).astype(jnp.float32)
    before = jnp.dot(lower, tok_oh, preferred_element_type=jnp.float32)
    slot_hit = before.T[:, None, :] == jnp.arange(slots, dtype=jnp.float32)[None, :, None]
    pick3 = slot_hit & (tok_oh.T[:, None, :] > 0)
    pick = pick3.reshape(rows_all, tok_count).astype(jnp.bfloat16)
    gate_tc = jnp.sum(hit_f * gate_weights.astype(jnp.float32)[:, :, None], axis=1)
    send_x = jnp.dot(pick, tokens, preferred_element_type=jnp.float32)
    send_dy = jnp.dot(pick, upstream, preferred_element_type=jnp.float32)
    send_gate = jnp.einsum(
        "cst,tc->cs", pick3.astype(jnp.float32), gate_tc, preferred_element_type=jnp.float32
    ).reshape(rows_all)
    gate_rows = jnp.pad(
        send_gate.reshape(owners, 1, slots), ((0, 0), (slots - 1, 0), (0, width - slots))
    ).reshape(rows_all, width)
    packed = jnp.concatenate([send_x, send_dy + gate_rows], axis=1).astype(jnp.bfloat16)
    recv = lax.all_to_all(
        packed.reshape(owners, slots, -1), "expert", 0, 0, tiled=True
    ).reshape(rows_all, -1)
    rows_x = recv[:, :width]
    rows_dy = recv[:, width : 2 * width]
    rows_gate = recv.reshape(owners, slots, -1)[:, slots - 1, width : width + slots].reshape(rows_all)
    act = jnp.dot(rows_x, up_mat, preferred_element_type=jnp.float32)
    sig = jax.nn.sigmoid(act)
    hidden = (act * sig).astype(jnp.bfloat16)
    expert_out = jnp.dot(hidden, down_mat, preferred_element_type=jnp.float32)
    dy_wide = rows_dy.astype(jnp.float32)
    gate_term = jnp.sum(dy_wide * expert_out, axis=1)
    local_col = jnp.sum(gate_term[:, None] * rows_x.astype(jnp.float32), axis=0)
    router_grads = dp_sum(local_col) / jnp.float32(column_tok)
    scaled = (rows_gate.astype(jnp.float32)[:, None] * dy_wide).astype(jnp.bfloat16)
    back = lax.dot_general(
        scaled, down_mat, (((1,), (1,)), ((), ())), preferred_element_type=jnp.float32
    )
    act_grad = (back * sig * (1.0 + act * (1.0 - sig))).astype(jnp.bfloat16)
    route_grad = lax.dot_general(
        act_grad, up_mat, (((1,), (1,)), ((), ())), preferred_element_type=jnp.float32
    ).astype(jnp.bfloat16)
    gate_back = jnp.pad(
        gate_term.astype(jnp.bfloat16).reshape(owners, 1, slots),
        ((0, 0), (slots - 1, 0), (0, width - slots)),
    ).reshape(rows_all, width)
    returned = lax.all_to_all(
        (route_grad + gate_back).reshape(owners, slots, -1),
        "expert",
        0,
        0,
        tiled=True,
    ).reshape(rows_all, -1)
    back_rows = returned
    back_gate = returned.reshape(owners, slots, -1)[:, slots - 1, :slots].astype(jnp.float32)
    token_grads = lax.dot_general(
        pick, back_rows, (((0,), (0,)), ((), ())), preferred_element_type=jnp.float32
    ).astype(jnp.bfloat16)
    gate_back_tc = jnp.einsum(
        "cst,cs->tc", pick3.astype(jnp.float32), back_gate, preferred_element_type=jnp.float32
    )
    gate_grads = jnp.sum(hit_f * gate_back_tc[:, None, :], axis=2).astype(jnp.bfloat16)
    return (token_grads, gate_grads, router_grads[None])


def solution(mesh):
    n_dp = mesh.shape["dp"]
    rows = ("far", "quad", "pair", "core", "expert")
    split = Mesh(
        mesh.devices.reshape(n_dp // 8, 2, 2, 2, mesh.shape["expert"]), rows
    )
    return jax.shard_map(
        body,
        mesh=split,
        in_specs=(
            P(rows, None),
            P(rows, None),
            P(rows, None),
            P(rows, None),
            P("expert", None, None),
            P("expert", None, None),
        ),
        out_specs=(P(rows, None), P(rows, None), P("expert", None)),
        check_vma=False,
    )
```

```python
import jax
import jax.numpy as jnp
from jax import lax
from jax.sharding import Mesh, PartitionSpec as P

EXP_DEV = 8


def dp_sum(local_col):
    return lax.psum(lax.psum(lax.psum(local_col, "core"), "near"), "far")


def body(tokens, upstream, expert_ids, gate_weights, w_up, w_down):
    owners = lax.axis_size("expert")
    experts = EXP_DEV * owners
    tok_count, top = expert_ids.shape
    width = tokens.shape[1]
    column_tok = tok_count * lax.axis_size(("far", "near", "core"))
    most = tok_count * top // experts + tok_count * top // (4 * experts)
    slots = -(-(most + 1) // 8) * 8
    rows_all = owners * slots
    up_mat = w_up[0]
    down_mat = w_down[0]
    hit = expert_ids[:, :, None] == (EXP_DEV * jnp.arange(owners))[None, None, :]
    hit_f = hit.astype(jnp.float32)
    tok_oh = jnp.sum(hit_f, axis=1)
    lower = (jnp.arange(tok_count)[None, :] < jnp.arange(tok_count)[:, None]).astype(jnp.float32)
    before = jnp.dot(lower, tok_oh, preferred_element_type=jnp.float32)
    slot_hit = before.T[:, None, :] == jnp.arange(slots, dtype=jnp.float32)[None, :, None]
    pick3 = slot_hit & (tok_oh.T[:, None, :] > 0)
    pick = pick3.reshape(rows_all, tok_count).astype(jnp.bfloat16)
    gate_tc = jnp.sum(hit_f * gate_weights.astype(jnp.float32)[:, :, None], axis=1)
    send_x = jnp.dot(pick, tokens, preferred_element_type=jnp.float32)
    send_dy = jnp.dot(pick, upstream, preferred_element_type=jnp.float32)
    send_gate = jnp.einsum(
        "cst,tc->cs", pick3.astype(jnp.float32), gate_tc, preferred_element_type=jnp.float32
    ).reshape(rows_all)
    gate_rows = jnp.pad(
        send_gate.reshape(owners, 1, slots), ((0, 0), (slots - 1, 0), (0, width - slots))
    ).reshape(rows_all, width)
    packed = jnp.concatenate([send_x, send_dy + gate_rows], axis=1).astype(jnp.bfloat16)
    recv = lax.all_to_all(
        packed.reshape(owners, slots, -1), "expert", 0, 0, tiled=True
    ).reshape(rows_all, -1)
    rows_x = recv[:, :width]
    rows_dy = recv[:, width : 2 * width]
    rows_gate = recv.reshape(owners, slots, -1)[:, slots - 1, width : width + slots].reshape(rows_all)
    act = jnp.dot(rows_x, up_mat, preferred_element_type=jnp.float32)
    sig = jax.nn.sigmoid(act)
    hidden = (act * sig).astype(jnp.bfloat16)
    expert_out = jnp.dot(hidden, down_mat, preferred_element_type=jnp.float32)
    dy_wide = rows_dy.astype(jnp.float32)
    gate_term = jnp.sum(dy_wide * expert_out, axis=1)
    local_col = jnp.sum(gate_term[:, None] * rows_x.astype(jnp.float32), axis=0)
    router_grads = dp_sum(local_col) / jnp.float32(column_tok)
    scaled = (rows_gate.astype(jnp.float32)[:, None] * dy_wide).astype(jnp.bfloat16)
    back = lax.dot_general(
        scaled, down_mat, (((1,), (1,)), ((), ())), preferred_element_type=jnp.float32
    )
    act_grad = (back * sig * (1.0 + act * (1.0 - sig))).astype(jnp.bfloat16)
    route_grad = lax.dot_general(
        act_grad, up_mat, (((1,), (1,)), ((), ())), preferred_element_type=jnp.float32
    ).astype(jnp.bfloat16)
    gate_back = jnp.pad(
        gate_term.astype(jnp.bfloat16).reshape(owners, 1, slots),
        ((0, 0), (slots - 1, 0), (0, width - slots)),
    ).reshape(rows_all, width)
    returned = lax.all_to_all(
        (route_grad + gate_back).reshape(owners, slots, -1),
        "expert",
        0,
        0,
        tiled=True,
    ).reshape(rows_all, -1)
    back_rows = returned
    back_gate = returned.reshape(owners, slots, -1)[:, slots - 1, :slots].astype(jnp.float32)
    token_grads = lax.dot_general(
        pick, back_rows, (((0,), (0,)), ((), ())), preferred_element_type=jnp.float32
    ).astype(jnp.bfloat16)
    gate_back_tc = jnp.einsum(
        "cst,cs->tc", pick3.astype(jnp.float32), back_gate, preferred_element_type=jnp.float32
    )
    gate_grads = jnp.sum(hit_f * gate_back_tc[:, None, :], axis=2).astype(jnp.bfloat16)
    return (token_grads, gate_grads, router_grads[None])


def solution(mesh):
    n_dp = mesh.shape["dp"]
    rows = ("far", "near", "core", "expert")
    split = Mesh(
        mesh.devices.reshape(n_dp // 8, 4, 2, mesh.shape["expert"]), rows
    )
    return jax.shard_map(
        body,
        mesh=split,
        in_specs=(
            P(rows, None),
            P(rows, None),
            P(rows, None),
            P(rows, None),
            P("expert", None, None),
            P("expert", None, None),
        ),
        out_specs=(P(rows, None), P(rows, None), P("expert", None)),
        check_vma=False,
    )
```

```python
import jax
import jax.numpy as jnp
from jax import lax
from jax.sharding import Mesh, PartitionSpec as P

EXP_DEV = 8


def dp_sum(local_col):
    return lax.psum(lax.psum(lax.psum(local_col, "core"), "near"), "far")


def body(tokens, upstream, expert_ids, gate_weights, w_up, w_down):
    owners = lax.axis_size("expert")
    experts = EXP_DEV * owners
    tok_count, top = expert_ids.shape
    width = tokens.shape[1]
    column_tok = tok_count * lax.axis_size(("far", "near", "core"))
    most = tok_count * top // experts + tok_count * top // (4 * experts)
    slots = -(-(most + 1) // 8) * 8
    rows_all = owners * slots
    up_mat = w_up[0]
    down_mat = w_down[0]
    hit = expert_ids[:, :, None] == (EXP_DEV * jnp.arange(owners))[None, None, :]
    hit_f = hit.astype(jnp.float32)
    tok_oh = jnp.sum(hit_f, axis=1)
    lower = (jnp.arange(tok_count)[None, :] < jnp.arange(tok_count)[:, None]).astype(jnp.float32)
    before = jnp.dot(lower, tok_oh, preferred_element_type=jnp.float32)
    slot_hit = before.T[:, None, :] == jnp.arange(slots, dtype=jnp.float32)[None, :, None]
    pick3 = slot_hit & (tok_oh.T[:, None, :] > 0)
    pick = pick3.reshape(rows_all, tok_count).astype(jnp.bfloat16)
    gate_tc = jnp.sum(
        jnp.where(hit, gate_weights[:, :, None], jnp.zeros((), gate_weights.dtype)), axis=1
    ).astype(jnp.float32)
    send_x = jnp.dot(pick, tokens, preferred_element_type=jnp.float32)
    send_dy = jnp.dot(pick, upstream, preferred_element_type=jnp.float32)
    send_gate = jnp.einsum(
        "cst,tc->cs", pick3.astype(jnp.float32), gate_tc, preferred_element_type=jnp.float32
    ).reshape(rows_all)
    gate_rows = jnp.pad(
        send_gate.reshape(owners, 1, slots), ((0, 0), (slots - 1, 0), (0, width - slots))
    ).reshape(rows_all, width)
    packed = jnp.concatenate([send_x, send_dy + gate_rows], axis=1).astype(jnp.bfloat16)
    recv = lax.all_to_all(
        packed.reshape(owners, slots, -1), "expert", 0, 0, tiled=True
    ).reshape(rows_all, -1)
    rows_x = recv[:, :width]
    rows_dy = recv[:, width : 2 * width]
    rows_gate = recv.reshape(owners, slots, -1)[:, slots - 1, width : width + slots].reshape(rows_all)
    act = jnp.dot(rows_x, up_mat, preferred_element_type=jnp.float32)
    sig = jax.nn.sigmoid(act)
    hidden = (act * sig).astype(jnp.bfloat16)
    expert_out = jnp.dot(hidden, down_mat, preferred_element_type=jnp.float32)
    dy_wide = rows_dy.astype(jnp.float32)
    gate_term = jnp.sum(dy_wide * expert_out, axis=1)
    local_col = jnp.sum(gate_term[:, None] * rows_x.astype(jnp.float32), axis=0)
    router_grads = dp_sum(local_col) / jnp.float32(column_tok)
    scaled = (rows_gate.astype(jnp.float32)[:, None] * dy_wide).astype(jnp.bfloat16)
    back = lax.dot_general(
        scaled, down_mat, (((1,), (1,)), ((), ())), preferred_element_type=jnp.float32
    )
    act_grad = (back * sig * (1.0 + act * (1.0 - sig))).astype(jnp.bfloat16)
    route_grad = lax.dot_general(
        act_grad, up_mat, (((1,), (1,)), ((), ())), preferred_element_type=jnp.float32
    ).astype(jnp.bfloat16)
    gate_back = jnp.pad(
        gate_term.astype(jnp.bfloat16).reshape(owners, 1, slots),
        ((0, 0), (slots - 1, 0), (0, width - slots)),
    ).reshape(rows_all, width)
    returned = lax.all_to_all(
        (route_grad + gate_back).reshape(owners, slots, -1),
        "expert",
        0,
        0,
        tiled=True,
    ).reshape(rows_all, -1)
    back_rows = returned
    back_gate = returned.reshape(owners, slots, -1)[:, slots - 1, :slots].astype(jnp.float32)
    token_grads = lax.dot_general(
        pick, back_rows, (((0,), (0,)), ((), ())), preferred_element_type=jnp.float32
    ).astype(jnp.bfloat16)
    gate_back_tc = jnp.einsum(
        "cst,cs->tc", pick3.astype(jnp.float32), back_gate, preferred_element_type=jnp.float32
    )
    gate_grads = jnp.sum(hit_f * gate_back_tc[:, None, :], axis=2).astype(jnp.bfloat16)
    return (token_grads, gate_grads, router_grads[None])


def solution(mesh):
    n_dp = mesh.shape["dp"]
    rows = ("far", "near", "core", "expert")
    split = Mesh(
        mesh.devices.reshape(n_dp // 8, 4, 2, mesh.shape["expert"]), rows
    )
    return jax.shard_map(
        body,
        mesh=split,
        in_specs=(
            P(rows, None),
            P(rows, None),
            P(rows, None),
            P(rows, None),
            P("expert", None, None),
            P("expert", None, None),
        ),
        out_specs=(P(rows, None), P(rows, None), P("expert", None)),
        check_vma=False,
    )
```
